32 devices in a mesh: front: 2 (over core), row: 4 (over z), col: 4 (over y, x).
Axes of the slice: x: 2, y: 2, z: 4, core: 2. Of those that a mesh axis runs over, the one named last changes fastest.
Arguments:
- panel: float32 [4096, 512], P(('front', 'row'), 'col'), as said below
- trailing: float32 [4096, 8192], P(('front', 'row'), 'col'), may hold values from -6 to 6
- pattern: int32 [32, 64], P(('front', 'row'), 'col'), may hold values 0 or 1
Outputs:
- r_panel: float32 [512, 512], P(None, 'col')
- r_trail: float32 [512, 8192], P(('front', 'row'), 'col')
- residual: float32 [4096, 8192], P(('front', 'row'), 'col')
The draws below stay inside these ranges and needn't reach their ends.
Inputs may be any that keep to these rules, and one draw needn't show every extreme that they name: Real-valued entries; the panel has full column rank.
All inputs are finite; a program needn't handle non-finite values. No bound on the sum of `pattern` on one device may be relied on, other than what follows from the above.
Results may differ from the reference program's by a relative error of at most 0.0003.
Values sent between devices are 32-bit elements; how exact they have to be, the bound alone decides.
No kernel may reach another device: no remote copies, remote signals or barrier semaphores. Data moves between devices by JAX's collectives and lax.ppermute only.
A program may use at most 64 MiB of HBM per device.

```python
import math
import jax
import jax.numpy as jnp
from jax import lax

BLK = 128
PW = 512
NT = 8192
ROWS = 4096


def draw_panel(key, part):
    key_main = jax.random.fold_in(key, 11)
    first, second, third = jax.random.split(key_main, 3)
    column_scale = jnp.exp(jax.random.uniform(first, (1, PW), jnp.float32, math.log(0.5), math.log(2.0)))
    shared = jax.random.normal(second, (ROWS, 1), jnp.float32)
    noise = jnp.clip(jax.random.normal(third, (ROWS, PW), jnp.float32), -6.0, 6.0)
    values = (noise + 0.6 * jnp.clip(shared, -6.0, 6.0)) * column_scale
    return (values * (1.0 / math.sqrt(ROWS))).astype(jnp.float32)


def with_ends(entries, rng, low, largest):
    index_at = [jax.random.randint(jax.random.fold_in(rng, axis), (), 0, length) for axis, length in enumerate(entries.shape)]
    widest = entries.shape.index(max(entries.shape))
    beside = index_at[:widest] + [(index_at[widest] + 1) % entries.shape[widest]] + index_at[widest + 1:]
    return entries.at[tuple(index_at)].set(low).at[tuple(beside)].set(largest)


def steps_of(key, extent, pieces, low, top_value):
    def one(dim, blocks):
        steps = jax.random.uniform(jax.random.fold_in(jax.random.fold_in(key, 6), dim), (blocks,), jnp.float32, low / len(pieces), top_value / len(pieces))
        return jnp.repeat(jnp.exp(steps), extent[dim] // blocks).reshape((-1,) + (1,) * (len(extent) - dim - 1))

    level = one(*pieces[0])
    for cut in pieces[1:]:
        level = level * one(*cut)
    return level


def normal_values(stream_key, shape, scale, reach, cuts=(), held_as=jnp.bfloat16):
    array = jax.random.normal(stream_key, shape, jnp.float32) * scale
    if len(cuts) > 0:
        array = steps_of(stream_key, shape, cuts, -0.22, 0.18) * array
    return jnp.clip(array, min=-reach, max=reach).astype(held_as)


def setup_inputs(seed: int = 0) -> dict:
    key_of = jax.random.split(jax.random.key(seed), 4)
    return {
        "panel": draw_panel(jax.random.fold_in(key_of[3], 71), 0),
        "trailing": normal_values(key_of[1], (ROWS, NT), 1.0, 6.0, ((0, 8), (1, 4)), jnp.float32),
        "pattern": with_ends((jax.random.randint(key_of[2], (ROWS // BLK, NT // BLK), 0, 4) < 3).astype(jnp.int32), jax.random.fold_in(key_of[2], 1), 0, 1),
    }


def reference(panel, trailing, pattern):
    mask = jnp.repeat(jnp.repeat(pattern.astype(jnp.float32), BLK, axis=0), BLK, axis=1)
    front = trailing * mask
    gram = jnp.dot(panel.T.astype(jnp.float32), panel.astype(jnp.float32), precision=lax.Precision.HIGHEST, preferred_element_type=jnp.float32)
    r_panel = jnp.linalg.cholesky(gram).T
    q_trans = lax.linalg.triangular_solve(r_panel, panel.T, left_side=True, lower=False, transpose_a=True)
    r_trail = jnp.dot(q_trans.astype(jnp.float32), front.astype(jnp.float32), precision=lax.Precision.HIGHEST, preferred_element_type=jnp.float32)
    residual = front - jnp.dot(q_trans.T.astype(jnp.float32), r_trail.astype(jnp.float32), precision=lax.Precision.HIGHEST, preferred_element_type=jnp.float32)
    return (r_panel, r_trail, residual)
```

```python
import jax
import jax.numpy as jnp
from jax import lax
from jax.sharding import PartitionSpec as P
from jax.experimental import pallas as pl
from jax.experimental.pallas import tpu as pltpu

BLK = 128
LEAF = 128


def contract_rows(left, right):
    return lax.dot_general(
        left,
        right,
        (((0,), (0,)), ((), ())),
        precision=lax.Precision.HIGHEST,
        preferred_element_type=jnp.float32,
    )


def product(left, right):
    return jnp.dot(left, right, precision=lax.Precision.HIGHEST, preferred_element_type=jnp.float32)


def product_trans(left, right):
    return lax.dot_general(
        left,
        right,
        (((1,), (1,)), ((), ())),
        precision=lax.Precision.HIGHEST,
        preferred_element_type=jnp.float32,
    )


def eliminate(work_ref):
    size = work_ref.shape[0]
    rows = lax.broadcasted_iota(jnp.int32, (size, 1), 0)
    lanes = lax.broadcasted_iota(jnp.int32, (1, size), 1)
    subs = lax.broadcasted_iota(jnp.int32, (8, 1), 0)

    for tile in range(size // 8):
        top = tile * 8
        rows_here = rows[top:]

        def step(j, carry, top=top, rows_here=rows_here):
            pick = subs == (j - top)
            left = work_ref[top:, :size]
            right = work_ref[top:, size:]
            pivot_left = jnp.sum(jnp.where(pick, left[:8], 0.0), axis=0, keepdims=True)
            pivot_right = jnp.sum(jnp.where(pick, right[:8], 0.0), axis=0, keepdims=True)
            pivot = jnp.sum(jnp.where(lanes == j, pivot_left, 0.0), axis=1, keepdims=True)
            scale = lax.rsqrt(pivot)
            scale = scale * (1.5 - 0.5 * pivot * scale * scale)
            row_left = pivot_left * scale
            row_right = pivot_right * scale
            column = jnp.sum(jnp.where(lanes == j, left, 0.0), axis=1, keepdims=True)
            mult = jnp.where(rows_here > j, column * scale, 0.0)
            new_left = left - mult * row_left
            new_right = right - mult * row_right
            work_ref[top:, :size] = jnp.where(rows_here == j, row_left, new_left)
            work_ref[top:, size:] = jnp.where(rows_here == j, row_right, new_right)
            return carry

        lax.fori_loop(top, top + 8, step, 0)


def identity(size):
    rows = lax.broadcasted_iota(jnp.int32, (size, size), 0)
    lanes = lax.broadcasted_iota(jnp.int32, (size, size), 1)
    return jnp.where(rows == lanes, 1.0, 0.0).astype(jnp.float32)


def leaf_kernel(a_ref, up_ref, inv_ref, work_ref):
    size = a_ref.shape[0]
    work_ref[:, :size] = a_ref[...]
    work_ref[:, size:] = identity(size)
    eliminate(work_ref)
    rows = lax.broadcasted_iota(jnp.int32, (size, size), 0)
    lanes = lax.broadcasted_iota(jnp.int32, (size, size), 1)
    up_ref[...] = jnp.where(rows <= lanes, work_ref[:, :size], 0.0)
    inv_ref[...] = jnp.where(rows >= lanes, work_ref[:, size:], 0.0)


def kernel_dot(left, right):
    return jnp.dot(left, right, precision=lax.Precision.HIGHEST, preferred_element_type=jnp.float32)


def kernel_dot_trans(left, right):
    return lax.dot_general(
        left, right, (((1,), (1,)), ((), ())), precision=lax.Precision.HIGHEST, preferred_element_type=jnp.float32
    )


def factor_kernel(g_ref, up_ref, inv_ref, work_ref, leaf_ref):
    order = g_ref.shape[0]
    count = order // LEAF
    work_ref[:, :order] = g_ref[...]
    work_ref[:, order:] = identity(order)
    small_rows = lax.broadcasted_iota(jnp.int32, (LEAF, LEAF), 0)
    small_lanes = lax.broadcasted_iota(jnp.int32, (LEAF, LEAF), 1)
    for k in range(count):
        low = k * LEAF
        high = low + LEAF
        leaf_ref[:, :LEAF] = work_ref[low:high, low:high]
        leaf_ref[:, LEAF:] = identity(LEAF)
        eliminate(leaf_ref)
        upper_kk = jnp.where(small_rows <= small_lanes, leaf_ref[:, :LEAF], 0.0)
        inverse_kk = jnp.where(small_rows >= small_lanes, leaf_ref[:, LEAF:], 0.0)
        scaled = kernel_dot(inverse_kk, work_ref[low:high, :])
        work_ref[low:high, :] = scaled
        work_ref[low:high, low:high] = upper_kk
        if k + 1 < count:
            mult = kernel_dot_trans(work_ref[high:, low:high], inverse_kk)
            work_ref[high:, :] = work_ref[high:, :] - kernel_dot(mult, scaled)
    rows = lax.broadcasted_iota(jnp.int32, (order, order), 0)
    lanes = lax.broadcasted_iota(jnp.int32, (order, order), 1)
    up_ref[...] = jnp.where(rows <= lanes, work_ref[:, :order], 0.0)
    inv_ref[...] = jnp.where(rows >= lanes, work_ref[:, order:], 0.0)


def factor_call(gram):
    order = gram.shape[0]
    return pl.pallas_call(
        factor_kernel,
        out_shape=(
            jax.ShapeDtypeStruct((order, order), jnp.float32),
            jax.ShapeDtypeStruct((order, order), jnp.float32),
        ),
        in_specs=[pl.BlockSpec(memory_space=pltpu.VMEM)],
        out_specs=(pl.BlockSpec(memory_space=pltpu.VMEM), pl.BlockSpec(memory_space=pltpu.VMEM)),
        scratch_shapes=[pltpu.VMEM((order, 2 * order), jnp.float32), pltpu.VMEM((LEAF, 2 * LEAF), jnp.float32)],
        cost_estimate=pl.CostEstimate(
            flops=8 * order * order * order, bytes_accessed=12 * order * order, transcendentals=order
        ),
    )(gram)


def leaf_call(block):
    size = block.shape[0]
    return pl.pallas_call(
        leaf_kernel,
        out_shape=(
            jax.ShapeDtypeStruct((size, size), jnp.float32),
            jax.ShapeDtypeStruct((size, size), jnp.float32),
        ),
        in_specs=[pl.BlockSpec(memory_space=pltpu.VMEM)],
        out_specs=(pl.BlockSpec(memory_space=pltpu.VMEM), pl.BlockSpec(memory_space=pltpu.VMEM)),
        scratch_shapes=[pltpu.VMEM((size, 2 * size), jnp.float32)],
        cost_estimate=pl.CostEstimate(flops=4 * size * size * size, bytes_accessed=12 * size * size, transcendentals=size),
    )(block)


def leaf_factor(block):
    upper, inverse = leaf_call(block)
    return upper.T, inverse


def factor_lower(gram):
    upper_full, inverse_full = factor_call(gram)
    return upper_full.T, inverse_full


def xor_pairs(count, shift):
    return [(i, i ^ shift) for i in range(count)]


def gather_cols(panel, axis):
    count = lax.axis_size(axis)
    if count & (count - 1):
        return lax.all_gather(panel, axis, axis=1, tiled=True)
    pieces = [panel]
    for shift in range(1, count):
        pieces.append(lax.ppermute(panel, axis, xor_pairs(count, shift)))
    stack = jnp.stack(pieces)
    index = lax.axis_index(axis)
    ordered = [lax.dynamic_index_in_dim(stack, index ^ j, 0, keepdims=False) for j in range(count)]
    return jnp.concatenate(ordered, axis=1)


def sum_over(value, axes):
    for axis in axes:
        count = lax.axis_size(axis)
        if count & (count - 1):
            value = lax.psum(value, axis)
            continue
        shift = 1
        while shift < count:
            value = value + lax.ppermute(value, axis, xor_pairs(count, shift))
            shift *= 2
    return value


def sum_gram(value, pair_axis, line_axis):
    pairs = lax.axis_size(pair_axis)
    if pairs != 2:
        return sum_over(value, (pair_axis, line_axis))
    half = value.shape[0] // 2
    mine = lax.axis_index(pair_axis)
    keep = lax.dynamic_slice_in_dim(value, mine * half, half, 0)
    give = lax.dynamic_slice_in_dim(value, (1 - mine) * half, half, 0)
    part = keep + lax.ppermute(give, pair_axis, [(0, 1), (1, 0)])
    part = sum_over(part, (line_axis,))
    other = lax.ppermute(part, pair_axis, [(0, 1), (1, 0)])
    first = jnp.where(mine == 0, part, other)
    second = jnp.where(mine == 0, other, part)
    return jnp.concatenate([first, second], axis=0)


def halving_sum(value, axes):
    sizes = [lax.axis_size(axis) for axis in axes]
    total = 1
    for size in sizes:
        total *= size
    if any(size & (size - 1) for size in sizes) or value.shape[0] % (8 * total):
        return sum_over(value, axes)
    steps = []
    for axis, size in zip(axes, sizes):
        index = lax.axis_index(axis)
        shift = 1
        while shift < size:
            steps.append((axis, size, shift, (index // shift) % 2))
            shift *= 2
    for axis, size, shift, bit in steps:
        half = value.shape[0] // 2
        keep = lax.dynamic_slice_in_dim(value, bit * half, half, 0)
        give = lax.dynamic_slice_in_dim(value, (1 - bit) * half, half, 0)
        value = keep + lax.ppermute(give, axis, xor_pairs(size, shift))
    for axis, size, shift, bit in reversed(steps):
        other = lax.ppermute(value, axis, xor_pairs(size, shift))
        first = jnp.where(bit == 0, value, other)
        second = jnp.where(bit == 0, other, value)
        value = jnp.concatenate([first, second], axis=0)
    return value


def on_device(panel, trailing, pattern):
    block_rows = pattern.shape[0]
    block_cols = pattern.shape[1]
    weights = pattern.astype(jnp.float32)[:, None, :, None]
    front = (trailing.reshape(block_rows, BLK, block_cols, BLK) * weights).reshape(trailing.shape)
    whole = gather_cols(panel, "col")
    gram_local = contract_rows(whole, whole)
    cross_local = contract_rows(whole, front)
    gram_local, cross_local = lax.optimization_barrier((gram_local, cross_local))
    gram = halving_sum(gram_local, ("front", "row"))
    cross = halving_sum(cross_local, ("front", "row"))
    lower_full, inverse_full = factor_lower(gram)
    q_local = product_trans(whole, inverse_full)
    upper_trail = product(inverse_full, cross)
    factor = lower_full.T
    residual = front - jnp.dot(q_local, upper_trail, precision=lax.Precision.HIGH, preferred_element_type=jnp.float32)
    col_count = lax.axis_size("col")
    col_width = factor.shape[1] // col_count
    factor_part = lax.dynamic_slice_in_dim(factor, lax.axis_index("col") * col_width, col_width, 1)
    group_count = lax.axis_size(("front", "row"))
    group_rows = upper_trail.shape[0] // group_count
    trail_part = lax.dynamic_slice_in_dim(
        upper_trail, lax.axis_index(("front", "row")) * group_rows, group_rows, 0
    )
    return (factor_part, trail_part, residual)


def solution(mesh):
    in_specs = (P(("front", "row"), "col"), P(("front", "row"), "col"), P(("front", "row"), "col"))
    out_specs = (P(None, "col"), P(("front", "row"), "col"), P(("front", "row"), "col"))
    return jax.shard_map(
        on_device, mesh=mesh, in_specs=in_specs, out_specs=out_specs, check_vma=False
    )
```
